256 devices in a mesh: svc: 32 (over y_lo, z, core), tm: 8 (over y_hi, x).
Axes of the slice: x: 4, y: 4 (y_hi: 2, y_lo: 2; y = y_hi * 2 + y_lo), z: 8, core: 2. Of those that a mesh axis runs over, the one named last changes fastest.
Arguments:
- metrics: bfloat16 [8192, 4096], P('svc', 'tm'), may hold values from -15 to 15
- band_starts: int32 [4], replicated, may hold values from 1 to 2015
Outputs:
- cross: bfloat16 [4, 2, 8192, 8192], P(None, None, 'svc', 'tm')
- coherence: float32 [4, 8192, 8192], P(None, 'svc', 'tm')
The draws below stay inside these ranges and needn't reach their ends.
Inputs may be any that keep to these rules, and one draw needn't show every extreme that they name: `band_starts`: each band covers 32 consecutive bins starting at its entry.
All inputs are finite; a program needn't handle non-finite values.
Results may differ from the reference program's by a relative error of at most 0.0066.
Values may be sent and summed in bfloat16 or wider, within the bound.
No kernel may reach another device: no remote copies, remote signals or barrier semaphores. Data moves between devices by JAX's collectives and lax.ppermute only.
A program may use at most 64 MiB of HBM per device.

```python
import jax
import jax.numpy as jnp
from jax import lax

CHANNELS = 8192
TLEN = 4096
BANDS = 4
BINS = 32


def draw_metrics(key, part):
    key_scale, key_base = jax.random.split(key, 2)
    scales = jnp.exp(jax.random.uniform(key_scale, (CHANNELS, 1), jnp.float32, jnp.log(0.3), jnp.log(3.0)))
    values = jnp.clip(jax.random.normal(key_base, (CHANNELS, TLEN), jnp.float32), -5.0, 5.0)
    return (scales * values).astype(jnp.bfloat16)


def plant(array, own_key, low, top_value):
    shape = array.shape
    index_at = [jax.random.randint(jax.random.fold_in(own_key, axis), (), 0, shape[axis]) for axis in range(len(shape))]
    array = array.at[tuple(index_at)].set(low)
    longest = shape.index(max(shape))
    index_at[longest] = (index_at[longest] + 1) % shape[longest]
    return array.at[tuple(index_at)].set(top_value)


def setup_inputs(seed: int = 0) -> dict:
    arg_keys = jax.random.split(jax.random.key(seed), 3)
    return {
        "metrics": draw_metrics(jax.random.fold_in(arg_keys[2], 71), 0),
        "band_starts": plant(jax.random.randint(arg_keys[1], (BANDS,), 1, TLEN // 2 - BINS), jax.random.fold_in(arg_keys[1], 1), 1, (TLEN // 2 - BINS) - 1).astype(jnp.int32),
    }


epsilon = 1e-06

def make_table(minutes, band_starts):
    offsets = jnp.arange(BINS, dtype=jnp.int32)
    freqs = band_starts.astype(jnp.int32)[:, None] + offsets[None, :]
    phase_index = minutes[:, None, None] * freqs[None, :, :] % TLEN
    phases = 2.0 * jnp.pi / TLEN * phase_index.astype(jnp.float32)
    norm = 1.0 / jnp.sqrt(jnp.float32(TLEN))
    stacked = jnp.stack([jnp.cos(phases) * norm, -jnp.sin(phases) * norm], axis=2)
    return stacked.reshape(minutes.shape[0], BANDS * 2 * BINS).astype(jnp.bfloat16)

def band_products(row_spec, col_spec):
    swapped = jnp.concatenate([row_spec[:, BINS:], -row_spec[:, :BINS]], axis=1)
    dims = (((1,), (1,)), ((), ()))
    real_part = lax.dot_general(row_spec, col_spec, dims, preferred_element_type=jnp.float32) / BINS
    imag_part = lax.dot_general(swapped, col_spec, dims, preferred_element_type=jnp.float32) / BINS
    row_power = lax.optimization_barrier(jnp.sum(jnp.square(row_spec.astype(jnp.float32)), axis=1)) / BINS
    col_power = lax.optimization_barrier(jnp.sum(jnp.square(col_spec.astype(jnp.float32)), axis=1)) / BINS
    coherence = (real_part * real_part + imag_part * imag_part) / ((row_power[:, None] + epsilon) * (col_power[None, :] + epsilon))
    cross = jnp.stack([real_part, imag_part], axis=0).astype(jnp.bfloat16)
    return (cross, coherence)

def reference(metrics, band_starts):
    minutes = jnp.arange(TLEN, dtype=jnp.int32)
    dft_table = make_table(minutes, band_starts)
    spectra = jnp.dot(metrics, dft_table, preferred_element_type=jnp.float32).astype(jnp.bfloat16)
    cross_list = []
    coherence_list = []
    for band in range(BANDS):
        offset = band * 2 * BINS
        block = spectra[:, offset:offset + 2 * BINS]
        cross, coherence = band_products(block, block)
        cross_list.append(cross)
        coherence_list.append(coherence)
    return (jnp.stack(cross_list, axis=0), jnp.stack(coherence_list, axis=0))
```

```python
import jax
import jax.numpy as jnp
from jax import lax
from jax.sharding import PartitionSpec as P

TLEN = 4096
BANDS = 4
BINS = 32


epsilon = 1e-06


def make_table(minutes, band_starts):
    offsets = jnp.arange(BINS, dtype=jnp.int32)
    freqs = band_starts[:, None] + offsets[None, :]
    phase_index = minutes[:, None, None] * freqs[None, :, :] % TLEN
    phases = 2.0 * jnp.pi / TLEN * phase_index.astype(jnp.float32)
    norm = 1.0 / jnp.sqrt(jnp.float32(TLEN))
    stacked = jnp.stack([jnp.cos(phases) * norm, -jnp.sin(phases) * norm], axis=2)
    return stacked.reshape(minutes.shape[0], BANDS * 2 * BINS).astype(jnp.bfloat16)


def band_products(row_spec, col_spec):
    swapped = jnp.concatenate([row_spec[:, BINS:], -row_spec[:, :BINS]], axis=1)
    dims = (((1,), (1,)), ((), ()))
    real_part = lax.dot_general(row_spec, col_spec, dims, preferred_element_type=jnp.float32) / BINS
    imag_part = lax.dot_general(swapped, col_spec, dims, preferred_element_type=jnp.float32) / BINS
    row_power = jnp.sum(jnp.square(row_spec.astype(jnp.float32)), axis=1) / BINS
    col_power = jnp.sum(jnp.square(col_spec.astype(jnp.float32)), axis=1) / BINS
    coherence = (real_part * real_part + imag_part * imag_part) / (
        (row_power[:, None] + epsilon) * (col_power[None, :] + epsilon)
    )
    cross = jnp.stack([real_part, imag_part], axis=0).astype(jnp.bfloat16)
    return (cross, coherence)


def body(metrics, band_starts):
    row_count = metrics.shape[0]
    local_minutes = metrics.shape[1]
    n_tm = lax.axis_size("tm")
    n_svc = lax.axis_size("svc")
    owners = n_svc // n_tm
    width = BANDS * 2 * BINS
    chunk = width // n_tm
    time_index = lax.axis_index("tm")
    minutes = time_index * local_minutes + jnp.arange(local_minutes, dtype=jnp.int32)
    dft_table = make_table(minutes, band_starts).reshape(local_minutes, n_tm, chunk)
    partial_value = jnp.einsum(
        "nt,tcb->cnb", metrics, dft_table, preferred_element_type=jnp.float32
    )
    piece = lax.psum_scatter(partial_value, "tm", scatter_dimension=0, tiled=True)
    piece = piece.astype(jnp.bfloat16)
    row_chunks = lax.all_gather(piece, "tm", axis=0, tiled=True)
    spectra = jnp.transpose(row_chunks, (1, 0, 2)).reshape(row_count, width)
    perm = []
    for s_src in range(n_svc):
        g_src, r_src = divmod(s_src, owners)
        for t_src in range(n_tm):
            s_dst = t_src * owners + r_src
            t_dst = g_src
            perm.append((s_src * n_tm + t_src, s_dst * n_tm + t_dst))
    moved = lax.ppermute(piece, ("svc", "tm"), perm)
    col_chunks = lax.all_gather(moved, "svc", axis=0, tiled=True)
    columns_panel = (
        col_chunks.reshape(n_tm, owners, row_count, chunk)
        .transpose(1, 2, 0, 3)
        .reshape(owners * row_count, width)
    )
    cross_list = []
    coherence_list = []
    for band in range(BANDS):
        offset = band * 2 * BINS
        row_spec = spectra[:, offset : offset + 2 * BINS]
        col_spec = columns_panel[:, offset : offset + 2 * BINS]
        cross, coherence = band_products(row_spec, col_spec)
        cross_list.append(cross)
        coherence_list.append(coherence)
    return (jnp.stack(cross_list, axis=0), jnp.stack(coherence_list, axis=0))


def solution(mesh):
    return jax.shard_map(
        body,
        mesh=mesh,
        in_specs=(P("svc", "tm"), P()),
        out_specs=(P(None, None, "svc", "tm"), P(None, "svc", "tm")),
        check_vma=False,
    )
```

```python
import jax
import jax.numpy as jnp
from jax import lax
from jax.sharding import PartitionSpec as P

TLEN = 4096
BANDS = 4
BINS = 32


epsilon = 1e-06


def make_table(minutes, band_starts):
    offsets = jnp.arange(BINS, dtype=jnp.int32)
    freqs = band_starts[:, None] + offsets[None, :]
    phase_index = minutes[:, None, None] * freqs[None, :, :] % TLEN
    phases = 2.0 * jnp.pi / TLEN * phase_index.astype(jnp.float32)
    norm = 1.0 / jnp.sqrt(jnp.float32(TLEN))
    stacked = jnp.stack([jnp.cos(phases) * norm, -jnp.sin(phases) * norm], axis=2)
    return stacked.reshape(minutes.shape[0], BANDS * 2 * BINS).astype(jnp.bfloat16)


def all_bands(row_spec, col_spec):
    swapped = jnp.concatenate([row_spec[..., BINS:], -row_spec[..., :BINS]], axis=-1)
    lhs = jnp.stack([row_spec, swapped], axis=1)
    cross_f32 = jnp.einsum("bpik,bjk->bpij", lhs, col_spec, preferred_element_type=jnp.float32) / BINS
    row_power = jnp.sum(jnp.square(row_spec.astype(jnp.float32)), axis=-1) / BINS
    col_power = jnp.sum(jnp.square(col_spec.astype(jnp.float32)), axis=-1) / BINS
    real_part = cross_f32[:, 0]
    imag_part = cross_f32[:, 1]
    coherence = (real_part * real_part + imag_part * imag_part) / (
        (row_power[:, :, None] + epsilon) * (col_power[:, None, :] + epsilon)
    )
    return (cross_f32.astype(jnp.bfloat16), coherence)


def gather_by_all_to_all(x, axis, size):
    return lax.all_to_all(jnp.broadcast_to(x, (size,) + x.shape[1:]), axis, 0, 0, tiled=True)


def body(metrics, band_starts):
    row_count = metrics.shape[0]
    local_minutes = metrics.shape[1]
    n_tm = lax.axis_size("tm")
    n_svc = lax.axis_size("svc")
    owners = n_svc // n_tm
    width = BANDS * 2 * BINS
    chunk = width // n_tm
    time_index = lax.axis_index("tm")
    minutes = time_index * local_minutes + jnp.arange(local_minutes, dtype=jnp.int32)
    dft_table = make_table(minutes, band_starts).reshape(local_minutes, n_tm, chunk)
    partial_value = jnp.einsum(
        "nt,tcb->cnb", metrics, dft_table, preferred_element_type=jnp.float32
    )
    partials = lax.all_to_all(partial_value, "tm", 0, 0, tiled=True)
    piece = jnp.sum(partials, axis=0, keepdims=True).astype(jnp.bfloat16)
    perm = []
    for s_src in range(n_svc):
        g_src, r_src = divmod(s_src, owners)
        for t_src in range(n_tm):
            s_dst = t_src * owners + r_src
            t_dst = g_src
            perm.append((s_src * n_tm + t_src, s_dst * n_tm + t_dst))
    moved = lax.ppermute(piece, ("svc", "tm"), perm)
    row_chunks = gather_by_all_to_all(piece, "tm", n_tm)
    col_chunks = gather_by_all_to_all(moved, "svc", n_svc)
    bands_row = row_chunks.reshape(BANDS, 2, row_count, BINS)
    row_spec = jnp.transpose(bands_row, (0, 2, 1, 3)).reshape(BANDS, row_count, 2 * BINS)
    bands_col = col_chunks.reshape(BANDS, 2, owners, row_count, BINS)
    col_spec = jnp.transpose(bands_col, (0, 2, 3, 1, 4)).reshape(BANDS, owners * row_count, 2 * BINS)
    return all_bands(row_spec, col_spec)


def solution(mesh):
    return jax.shard_map(
        body,
        mesh=mesh,
        in_specs=(P("svc", "tm"), P()),
        out_specs=(P(None, None, "svc", "tm"), P(None, "svc", "tm")),
        check_vma=False,
    )
```

```python
import jax
import jax.numpy as jnp
from jax import lax
from jax.experimental import pallas as pl
from jax.experimental.pallas import tpu as pltpu
from jax.sharding import PartitionSpec as P

TLEN = 4096
BANDS = 4
BINS = 32


epsilon = 1e-06


def make_table(minutes, band_starts):
    offsets = jnp.arange(BINS, dtype=jnp.int32)
    freqs = band_starts[:, None] + offsets[None, :]
    phase_index = minutes[:, None, None] * freqs[None, :, :] % TLEN
    phases = 2.0 * jnp.pi / TLEN * phase_index.astype(jnp.float32)
    norm = 1.0 / jnp.sqrt(jnp.float32(TLEN))
    stacked = jnp.stack([jnp.cos(phases) * norm, -jnp.sin(phases) * norm], axis=2)
    return stacked.reshape(minutes.shape[0], BANDS * 2 * BINS).astype(jnp.bfloat16)


def cross_kernel(row_ref, col_ref, row_power_ref, col_power_ref, cross_ref, coherence_ref):
    row_re = row_ref[0]
    row_im = row_ref[1]
    col_re = col_ref[0]
    col_im = col_ref[1]
    dims = (((1,), (1,)), ((), ()))

    def dot(a, b):
        return lax.dot_general(a, b, dims, preferred_element_type=jnp.float32)

    real_part = (dot(row_re, col_re) + dot(row_im, col_im)) / BINS
    imag_part = (dot(row_im, col_re) - dot(row_re, col_im)) / BINS
    cross_ref[0, 0] = real_part.astype(cross_ref.dtype)
    cross_ref[0, 1] = imag_part.astype(cross_ref.dtype)
    coherence_ref[0] = (real_part * real_part + imag_part * imag_part) / (
        (row_power_ref[0] + epsilon) * (col_power_ref[0] + epsilon)
    )


def all_bands(row_chunks, col_chunks):
    parts, rows, bins = row_chunks.shape
    cols = col_chunks.shape[1]
    bands = parts // 2
    tile = 128
    row_power = jnp.sum(
        jnp.square(row_chunks.astype(jnp.float32)).reshape(bands, 2, rows, bins), axis=(1, 3)
    ) / BINS
    col_power = jnp.sum(
        jnp.square(col_chunks.astype(jnp.float32)).reshape(bands, 2, cols, bins), axis=(1, 3)
    ) / BINS
    return pl.pallas_call(
        cross_kernel,
        grid=(bands, rows // tile),
        in_specs=[
            pl.BlockSpec((2, tile, bins), lambda b, i: (b, i, 0)),
            pl.BlockSpec((2, cols, bins), lambda b, i: (b, 0, 0)),
            pl.BlockSpec((1, tile, 1), lambda b, i: (b, i, 0)),
            pl.BlockSpec((1, 1, cols), lambda b, i: (b, 0, 0)),
        ],
        out_specs=[
            pl.BlockSpec((1, 2, tile, cols), lambda b, i: (b, 0, i, 0)),
            pl.BlockSpec((1, tile, cols), lambda b, i: (b, i, 0)),
        ],
        out_shape=[
            jax.ShapeDtypeStruct((bands, 2, rows, cols), jnp.bfloat16),
            jax.ShapeDtypeStruct((bands, rows, cols), jnp.float32),
        ],
        cost_estimate=pl.CostEstimate(
            flops=8 * bands * rows * cols * bins + 6 * bands * rows * cols,
            transcendentals=0,
            bytes_accessed=6 * bands * rows * cols,
        ),
    )(row_chunks, col_chunks, row_power[:, :, None], col_power[:, None, :])


def gather_by_all_to_all(x, axis, size):
    return lax.all_to_all(jnp.broadcast_to(x, (size,) + x.shape[1:]), axis, 0, 0, tiled=True)


def body(metrics, band_starts):
    row_count = metrics.shape[0]
    local_minutes = metrics.shape[1]
    n_tm = lax.axis_size("tm")
    n_svc = lax.axis_size("svc")
    owners = n_svc // n_tm
    width = BANDS * 2 * BINS
    chunk = width // n_tm
    time_index = lax.axis_index("tm")
    minutes = time_index * local_minutes + jnp.arange(local_minutes, dtype=jnp.int32)
    dft_table = make_table(minutes, band_starts).reshape(local_minutes, n_tm, chunk)
    partial_value = jnp.einsum(
        "nt,tcb->cnb", metrics, dft_table, preferred_element_type=jnp.float32
    )
    partials = lax.all_to_all(partial_value, "tm", 0, 0, tiled=True)
    piece = jnp.sum(partials, axis=0, keepdims=True).astype(jnp.bfloat16)
    perm = []
    for s_src in range(n_svc):
        g_src, r_src = divmod(s_src, owners)
        for t_src in range(n_tm):
            s_dst = t_src * owners + r_src
            t_dst = g_src
            perm.append((s_src * n_tm + t_src, s_dst * n_tm + t_dst))
    moved = lax.ppermute(piece, ("svc", "tm"), perm)
    row_chunks = gather_by_all_to_all(piece, "tm", n_tm)
    col_chunks = gather_by_all_to_all(moved, "svc", n_svc)
    col_chunks = col_chunks.reshape(n_tm, owners * row_count, chunk)
    return all_bands(row_chunks, col_chunks)


def solution(mesh):
    return jax.shard_map(
        body,
        mesh=mesh,
        in_specs=(P("svc", "tm"), P()),
        out_specs=(P(None, None, "svc", "tm"), P(None, "svc", "tm")),
        check_vma=False,
    )
```

```python
import jax
import jax.numpy as jnp
from jax import lax
from jax.experimental import pallas as pl
from jax.experimental.pallas import tpu as pltpu
from jax.sharding import PartitionSpec as P

TLEN = 4096
BANDS = 4
BINS = 32


epsilon = 1e-06


def make_table(minutes, band_starts):
    offsets = jnp.arange(BINS, dtype=jnp.int32)
    freqs = band_starts[:, None] + offsets[None, :]
    phase_index = minutes[:, None, None] * freqs[None, :, :] % TLEN
    phases = 2.0 * jnp.pi / TLEN * phase_index.astype(jnp.float32)
    norm = 1.0 / jnp.sqrt(jnp.float32(TLEN))
    stacked = jnp.stack([jnp.cos(phases) * norm, -jnp.sin(phases) * norm], axis=2)
    return stacked.reshape(minutes.shape[0], BANDS * 2 * BINS).astype(jnp.bfloat16)


def cross_kernel(row_ref, col_ref, cross_ref, coherence_ref):
    row_re = row_ref[0].astype(jnp.float32)
    row_im = row_ref[1].astype(jnp.float32)
    col_re = col_ref[0].astype(jnp.float32)
    col_im = col_ref[1].astype(jnp.float32)

    def dot(a, b):
        return jnp.dot(a, b, preferred_element_type=jnp.float32)

    real_part = (dot(row_ref[0], col_ref[0]) + dot(row_ref[1], col_ref[1])) / BINS
    imag_part = (dot(row_ref[1], col_ref[0]) - dot(row_ref[0], col_ref[1])) / BINS
    row_power = (
        jnp.sum(row_re * row_re, axis=1, keepdims=True) + jnp.sum(row_im * row_im, axis=1, keepdims=True)
    ) / BINS
    col_power = (
        jnp.sum(col_re * col_re, axis=0, keepdims=True) + jnp.sum(col_im * col_im, axis=0, keepdims=True)
    ) / BINS
    cross_ref[0, 0] = real_part.astype(cross_ref.dtype)
    cross_ref[0, 1] = imag_part.astype(cross_ref.dtype)
    coherence_ref[0] = (real_part * real_part + imag_part * imag_part) / (
        (row_power + epsilon) * (col_power + epsilon)
    )


def all_bands(row_chunks, col_chunks):
    parts, rows, bins = row_chunks.shape
    cols = col_chunks.shape[2]
    bands = parts // 2
    tile = 128
    return pl.pallas_call(
        cross_kernel,
        grid=(bands, rows // tile),
        in_specs=[
            pl.BlockSpec((2, tile, bins), lambda b, i: (b, i, 0)),
            pl.BlockSpec((2, bins, cols), lambda b, i: (b, 0, 0)),
        ],
        out_specs=[
            pl.BlockSpec((1, 2, tile, cols), lambda b, i: (b, 0, i, 0)),
            pl.BlockSpec((1, tile, cols), lambda b, i: (b, i, 0)),
        ],
        out_shape=[
            jax.ShapeDtypeStruct((bands, 2, rows, cols), jnp.bfloat16),
            jax.ShapeDtypeStruct((bands, rows, cols), jnp.float32),
        ],
        cost_estimate=pl.CostEstimate(
            flops=8 * bands * rows * cols * bins + 6 * bands * rows * cols,
            transcendentals=0,
            bytes_accessed=6 * bands * rows * cols,
        ),
    )(row_chunks, col_chunks)


def gather_by_all_to_all(x, axis, size):
    return lax.all_to_all(jnp.broadcast_to(x, (size,) + x.shape[1:]), axis, 0, 0, tiled=True)


def body(metrics, band_starts):
    row_count = metrics.shape[0]
    local_minutes = metrics.shape[1]
    n_tm = lax.axis_size("tm")
    n_svc = lax.axis_size("svc")
    owners = n_svc // n_tm
    width = BANDS * 2 * BINS
    chunk = width // n_tm
    time_index = lax.axis_index("tm")
    minutes = time_index * local_minutes + jnp.arange(local_minutes, dtype=jnp.int32)
    dft_table = make_table(minutes, band_starts).reshape(local_minutes, n_tm, chunk)
    partial_value = jnp.einsum(
        "nt,tcb->cnb", metrics, dft_table, preferred_element_type=jnp.float32
    )
    partials = lax.all_to_all(partial_value, "tm", 0, 0, tiled=True)
    piece = jnp.sum(partials, axis=0, keepdims=True).astype(jnp.bfloat16)
    perm = []
    for s_src in range(n_svc):
        g_src, r_src = divmod(s_src, owners)
        for t_src in range(n_tm):
            s_dst = t_src * owners + r_src
            t_dst = g_src
            perm.append((s_src * n_tm + t_src, s_dst * n_tm + t_dst))
    moved = lax.ppermute(piece, ("svc", "tm"), perm)
    row_chunks = gather_by_all_to_all(piece, "tm", n_tm)
    col_chunks = gather_by_all_to_all(moved, "svc", n_svc)
    col_chunks = jnp.swapaxes(col_chunks.reshape(n_tm, owners * row_count, chunk), 1, 2)
    return all_bands(row_chunks, col_chunks)


def solution(mesh):
    return jax.shard_map(
        body,
        mesh=mesh,
        in_specs=(P("svc", "tm"), P()),
        out_specs=(P(None, None, "svc", "tm"), P(None, "svc", "tm")),
        check_vma=False,
    )
```

```python
import jax
import jax.numpy as jnp
from jax import lax
from jax.experimental import pallas as pl
from jax.experimental.pallas import tpu as pltpu
from jax.sharding import PartitionSpec as P

TLEN = 4096
BANDS = 4
BINS = 32


epsilon = 1e-06


def make_table(minutes, band_starts):
    offsets = jnp.arange(BINS, dtype=jnp.int32)
    freqs = band_starts[:, None] + offsets[None, :]
    phase_index = minutes[:, None, None] * freqs[None, :, :] % TLEN
    phases = 2.0 * jnp.pi / TLEN * phase_index.astype(jnp.float32)
    norm = 1.0 / jnp.sqrt(jnp.float32(TLEN))
    stacked = jnp.stack([jnp.cos(phases) * norm, -jnp.sin(phases) * norm], axis=2)
    return stacked.reshape(minutes.shape[0], BANDS * 2 * BINS).astype(jnp.bfloat16)


def cross_kernel(lhs_ref, rhs_ref, cross_ref, coherence_ref):
    row_spec = lhs_ref[0, 0]
    col_spec = rhs_ref[0]
    real_part = jnp.dot(row_spec, col_spec, preferred_element_type=jnp.float32) / BINS
    imag_part = jnp.dot(lhs_ref[0, 1], col_spec, preferred_element_type=jnp.float32) / BINS
    row_values = row_spec.astype(jnp.float32)
    col_values = col_spec.astype(jnp.float32)
    row_power = jnp.sum(row_values * row_values, axis=1, keepdims=True) / BINS
    col_power = jnp.sum(col_values * col_values, axis=0, keepdims=True) / BINS
    cross_ref[0, 0] = real_part.astype(cross_ref.dtype)
    cross_ref[0, 1] = imag_part.astype(cross_ref.dtype)
    coherence_ref[0] = (real_part * real_part + imag_part * imag_part) / (
        (row_power + epsilon) * (col_power + epsilon)
    )


def all_bands(row_spec, col_spec):
    bands, rows, depth = row_spec.shape
    cols = col_spec.shape[2]
    swapped = jnp.concatenate([row_spec[..., BINS:], -row_spec[..., :BINS]], axis=-1)
    lhs = jnp.stack([row_spec, swapped], axis=1)
    tile = 128
    return pl.pallas_call(
        cross_kernel,
        grid=(bands, rows // tile),
        in_specs=[
            pl.BlockSpec((1, 2, tile, depth), lambda b, i: (b, 0, i, 0)),
            pl.BlockSpec((1, depth, cols), lambda b, i: (b, 0, 0)),
        ],
        out_specs=[
            pl.BlockSpec((1, 2, tile, cols), lambda b, i: (b, 0, i, 0)),
            pl.BlockSpec((1, tile, cols), lambda b, i: (b, i, 0)),
        ],
        out_shape=[
            jax.ShapeDtypeStruct((bands, 2, rows, cols), jnp.bfloat16),
            jax.ShapeDtypeStruct((bands, rows, cols), jnp.float32),
        ],
        cost_estimate=pl.CostEstimate(
            flops=4 * bands * rows * cols * depth + 6 * bands * rows * cols,
            transcendentals=0,
            bytes_accessed=6 * bands * rows * cols,
        ),
    )(lhs, col_spec)


def gather_by_all_to_all(x, axis, size):
    return lax.all_to_all(jnp.broadcast_to(x, (size,) + x.shape[1:]), axis, 0, 0, tiled=True)


def body(metrics, band_starts):
    row_count = metrics.shape[0]
    local_minutes = metrics.shape[1]
    n_tm = lax.axis_size("tm")
    n_svc = lax.axis_size("svc")
    owners = n_svc // n_tm
    width = BANDS * 2 * BINS
    chunk = width // n_tm
    time_index = lax.axis_index("tm")
    minutes = time_index * local_minutes + jnp.arange(local_minutes, dtype=jnp.int32)
    dft_table = make_table(minutes, band_starts).reshape(local_minutes, n_tm, chunk)
    partial_value = jnp.einsum(
        "nt,tcb->cnb", metrics, dft_table, preferred_element_type=jnp.float32
    )
    partials = lax.all_to_all(partial_value, "tm", 0, 0, tiled=True)
    piece = jnp.sum(partials, axis=0, keepdims=True).astype(jnp.bfloat16)
    perm = []
    for s_src in range(n_svc):
        g_src, r_src = divmod(s_src, owners)
        for t_src in range(n_tm):
            s_dst = t_src * owners + r_src
            t_dst = g_src
            perm.append((s_src * n_tm + t_src, s_dst * n_tm + t_dst))
    moved = lax.ppermute(piece, ("svc", "tm"), perm)
    row_chunks = gather_by_all_to_all(piece, "tm", n_tm)
    col_chunks = gather_by_all_to_all(moved, "svc", n_svc)
    bands_row = row_chunks.reshape(BANDS, 2, row_count, BINS)
    row_spec = jnp.transpose(bands_row, (0, 2, 1, 3)).reshape(BANDS, row_count, 2 * BINS)
    col_spec = jnp.swapaxes(col_chunks.reshape(BANDS, 2, owners * row_count, BINS), 2, 3)
    col_spec = col_spec.reshape(BANDS, 2 * BINS, owners * row_count)
    return all_bands(row_spec, col_spec)


def solution(mesh):
    return jax.shard_map(
        body,
        mesh=mesh,
        in_specs=(P("svc", "tm"), P()),
        out_specs=(P(None, None, "svc", "tm"), P(None, "svc", "tm")),
        check_vma=False,
    )
```

```python
import jax
import jax.numpy as jnp
from jax import lax
from jax.experimental import pallas as pl
from jax.experimental.pallas import tpu as pltpu
from jax.sharding import PartitionSpec as P

TLEN = 4096
BANDS = 4
BINS = 32


epsilon = 1e-06


def make_table(minutes, band_starts):
    offsets = jnp.arange(BINS, dtype=jnp.int32)
    freqs = band_starts[:, None] + offsets[None, :]
    phase_index = minutes[:, None, None] * freqs[None, :, :] % TLEN
    phases = 2.0 * jnp.pi / TLEN * phase_index.astype(jnp.float32)
    norm = 1.0 / jnp.sqrt(jnp.float32(TLEN))
    stacked = jnp.stack([jnp.cos(phases) * norm, -jnp.sin(phases) * norm], axis=2)
    return stacked.reshape(minutes.shape[0], BANDS * 2 * BINS).astype(jnp.bfloat16)


def cross_kernel(lhs_ref, rhs_ref, cross_ref, coherence_ref):
    row_spec = lhs_ref[0, 0]
    col_spec = rhs_ref[0]
    scale = 1.0 / BINS
    real_part = jnp.dot(row_spec, col_spec, preferred_element_type=jnp.float32) * scale
    imag_part = jnp.dot(lhs_ref[0, 1], col_spec, preferred_element_type=jnp.float32) * scale
    row_values = row_spec.astype(jnp.float32)
    col_values = col_spec.astype(jnp.float32)
    row_power = jnp.sum(row_values * row_values, axis=1, keepdims=True) * scale
    col_power = jnp.sum(col_values * col_values, axis=0, keepdims=True) * scale
    cross_ref[0, 0] = real_part.astype(cross_ref.dtype)
    cross_ref[0, 1] = imag_part.astype(cross_ref.dtype)
    row_inverse = 1.0 / (row_power + epsilon)
    col_inverse = 1.0 / (col_power + epsilon)
    coherence_ref[0] = (real_part * real_part + imag_part * imag_part) * row_inverse * col_inverse


def all_bands(row_spec, col_spec):
    bands, rows, depth = row_spec.shape
    cols = col_spec.shape[2]
    swapped = jnp.concatenate([row_spec[..., BINS:], -row_spec[..., :BINS]], axis=-1)
    lhs = jnp.stack([row_spec, swapped], axis=1)
    tile = 128
    return pl.pallas_call(
        cross_kernel,
        grid=(bands, rows // tile),
        in_specs=[
            pl.BlockSpec((1, 2, tile, depth), lambda b, i: (b, 0, i, 0)),
            pl.BlockSpec((1, depth, cols), lambda b, i: (b, 0, 0)),
        ],
        out_specs=[
            pl.BlockSpec((1, 2, tile, cols), lambda b, i: (b, 0, i, 0)),
            pl.BlockSpec((1, tile, cols), lambda b, i: (b, i, 0)),
        ],
        out_shape=[
            jax.ShapeDtypeStruct((bands, 2, rows, cols), jnp.bfloat16),
            jax.ShapeDtypeStruct((bands, rows, cols), jnp.float32),
        ],
        cost_estimate=pl.CostEstimate(
            flops=4 * bands * rows * cols * depth + 6 * bands * rows * cols,
            transcendentals=0,
            bytes_accessed=6 * bands * rows * cols,
        ),
    )(lhs, col_spec)


def gather_by_all_to_all(x, axis, size):
    return lax.all_to_all(jnp.broadcast_to(x, (size,) + x.shape[1:]), axis, 0, 0, tiled=True)


def body(metrics, band_starts):
    row_count = metrics.shape[0]
    local_minutes = metrics.shape[1]
    n_tm = lax.axis_size("tm")
    n_svc = lax.axis_size("svc")
    owners = n_svc // n_tm
    width = BANDS * 2 * BINS
    chunk = width // n_tm
    time_index = lax.axis_index("tm")
    minutes = time_index * local_minutes + jnp.arange(local_minutes, dtype=jnp.int32)
    dft_table = make_table(minutes, band_starts).reshape(local_minutes, n_tm, chunk)
    partial_value = jnp.einsum(
        "nt,tcb->cnb", metrics, dft_table, preferred_element_type=jnp.float32
    )
    partials = lax.all_to_all(partial_value, "tm", 0, 0, tiled=True)
    piece = jnp.sum(partials, axis=0, keepdims=True).astype(jnp.bfloat16)
    perm = []
    for s_src in range(n_svc):
        g_src, r_src = divmod(s_src, owners)
        for t_src in range(n_tm):
            s_dst = t_src * owners + r_src
            t_dst = g_src
            perm.append((s_src * n_tm + t_src, s_dst * n_tm + t_dst))
    moved = lax.ppermute(piece, ("svc", "tm"), perm)
    row_chunks = gather_by_all_to_all(piece, "tm", n_tm)
    col_chunks = gather_by_all_to_all(moved, "svc", n_svc)
    bands_row = row_chunks.reshape(BANDS, 2, row_count, BINS)
    row_spec = jnp.transpose(bands_row, (0, 2, 1, 3)).reshape(BANDS, row_count, 2 * BINS)
    col_spec = jnp.swapaxes(col_chunks.reshape(BANDS, 2, owners * row_count, BINS), 2, 3)
    col_spec = col_spec.reshape(BANDS, 2 * BINS, owners * row_count)
    return all_bands(row_spec, col_spec)


def solution(mesh):
    return jax.shard_map(
        body,
        mesh=mesh,
        in_specs=(P("svc", "tm"), P()),
        out_specs=(P(None, None, "svc", "tm"), P(None, "svc", "tm")),
        check_vma=False,
    )
```

```python
import jax
import jax.numpy as jnp
from jax import lax
from jax.sharding import PartitionSpec as P

TLEN = 4096
BANDS = 4
BINS = 32


epsilon = 1e-06


def make_table(minutes, band_starts):
    offsets = jnp.arange(BINS, dtype=jnp.int32)
    freqs = band_starts[:, None] + offsets[None, :]
    phase_index = minutes[:, None, None] * freqs[None, :, :] % TLEN
    phases = 2.0 * jnp.pi / TLEN * phase_index.astype(jnp.float32)
    norm = 1.0 / jnp.sqrt(jnp.float32(TLEN))
    stacked = jnp.stack([jnp.cos(phases) * norm, -jnp.sin(phases) * norm], axis=2)
    return stacked.reshape(minutes.shape[0], BANDS * 2 * BINS).astype(jnp.bfloat16)


def all_bands(row_spec, col_spec):
    swapped = jnp.concatenate([row_spec[..., BINS:], -row_spec[..., :BINS]], axis=-1)
    lhs = jnp.stack([row_spec, swapped], axis=1)
    cross_f32 = jnp.einsum("bpik,bjk->bpij", lhs, col_spec, preferred_element_type=jnp.float32) / BINS
    row_power = jnp.sum(jnp.square(row_spec.astype(jnp.float32)), axis=-1) / BINS
    col_power = jnp.sum(jnp.square(col_spec.astype(jnp.float32)), axis=-1) / BINS
    real_part = cross_f32[:, 0]
    imag_part = cross_f32[:, 1]
    coherence = (real_part * real_part + imag_part * imag_part) / (
        (row_power[:, :, None] + epsilon) * (col_power[:, None, :] + epsilon)
    )
    return (cross_f32.astype(jnp.bfloat16), coherence)


def gather_by_all_to_all(x, axis, size):
    return lax.all_to_all(jnp.broadcast_to(x, (size,) + x.shape[1:]), axis, 0, 0, tiled=True)


def body(metrics, band_starts):
    row_count = metrics.shape[0]
    local_minutes = metrics.shape[1]
    n_tm = lax.axis_size("tm")
    n_svc = lax.axis_size(SVC)
    owners = n_svc // n_tm
    width = BANDS * 2 * BINS
    chunk = width // n_tm
    time_index = lax.axis_index("tm")
    minutes = time_index * local_minutes + jnp.arange(local_minutes, dtype=jnp.int32)
    dft_table = make_table(minutes, band_starts).reshape(local_minutes, n_tm, chunk)
    partial_value = jnp.einsum(
        "nt,tcb->cnb", metrics, dft_table, preferred_element_type=jnp.float32
    )
    partials = lax.all_to_all(partial_value, "tm", 0, 0, tiled=True)
    piece = jnp.sum(partials, axis=0, keepdims=True).astype(jnp.bfloat16)
    perm = []
    for s_src in range(n_svc):
        g_src, r_src = divmod(s_src, owners)
        for t_src in range(n_tm):
            s_dst = t_src * owners + r_src
            t_dst = g_src
            perm.append((s_src * n_tm + t_src, s_dst * n_tm + t_dst))
    moved = lax.ppermute(piece, SVC + ("tm",), perm)
    row_chunks = gather_by_all_to_all(piece, "tm", n_tm)
    by_group = gather_by_all_to_all(moved, "group", n_svc // owners)
    by_owner = lax.all_to_all(jnp.broadcast_to(by_group[None], (owners,) + by_group.shape), "owner", 0, 0, tiled=True)
    col_chunks = jnp.swapaxes(by_owner, 0, 1).reshape((n_svc,) + moved.shape[1:])
    bands_row = row_chunks.reshape(BANDS, 2, row_count, BINS)
    row_spec = jnp.transpose(bands_row, (0, 2, 1, 3)).reshape(BANDS, row_count, 2 * BINS)
    bands_col = col_chunks.reshape(BANDS, 2, owners, row_count, BINS)
    col_spec = jnp.transpose(bands_col, (0, 2, 3, 1, 4)).reshape(BANDS, owners * row_count, 2 * BINS)
    return all_bands(row_spec, col_spec)


SVC = ("group", "owner")


def solution(mesh):
    n_svc, n_tm = mesh.shape["svc"], mesh.shape["tm"]
    owners = n_svc // n_tm
    split = jax.sharding.Mesh(mesh.devices.reshape(n_svc // owners, owners, n_tm), SVC + ("tm",))
    return jax.shard_map(
        body,
        mesh=split,
        in_specs=(P(SVC, "tm"), P()),
        out_specs=(P(None, None, SVC, "tm"), P(None, SVC, "tm")),
        check_vma=False,
    )
```

```python
import jax
import jax.numpy as jnp
from jax import lax
from jax.sharding import PartitionSpec as P

TLEN = 4096
BANDS = 4
BINS = 32


epsilon = 1e-06


def unit_phasors(minutes, freqs):
    phase_index = minutes[:, None, None] * freqs[None, :, :] % TLEN
    phases = 2.0 * jnp.pi / TLEN * phase_index.astype(jnp.float32)
    return jnp.cos(phases), jnp.sin(phases)


def make_table(first_minute, count, band_starts):
    offsets = jnp.arange(BINS, dtype=jnp.int32)
    freqs = band_starts[:, None] + offsets[None, :]
    step = 64
    fine_cos, fine_sin = unit_phasors(first_minute + jnp.arange(step, dtype=jnp.int32), freqs)
    coarse_cos, coarse_sin = unit_phasors(step * jnp.arange(count // step, dtype=jnp.int32), freqs)
    cos_value = coarse_cos[:, None] * fine_cos[None] - coarse_sin[:, None] * fine_sin[None]
    sin_value = coarse_sin[:, None] * fine_cos[None] + coarse_cos[:, None] * fine_sin[None]
    norm = 1.0 / jnp.sqrt(jnp.float32(TLEN))
    stacked = jnp.stack([cos_value * norm, -sin_value * norm], axis=3)
    return stacked.reshape(count, BANDS * 2 * BINS).astype(jnp.bfloat16)


def all_bands(row_spec, col_spec):
    swapped = jnp.concatenate([row_spec[..., BINS:], -row_spec[..., :BINS]], axis=-1)
    lhs = jnp.stack([row_spec, swapped], axis=1)
    cross_f32 = jnp.einsum("bpik,bjk->bpij", lhs, col_spec, preferred_element_type=jnp.float32) / BINS
    row_power = jnp.sum(jnp.square(row_spec.astype(jnp.float32)), axis=-1) / BINS
    col_power = jnp.sum(jnp.square(col_spec.astype(jnp.float32)), axis=-1) / BINS
    real_part = cross_f32[:, 0]
    imag_part = cross_f32[:, 1]
    coherence = (real_part * real_part + imag_part * imag_part) / (
        (row_power[:, :, None] + epsilon) * (col_power[:, None, :] + epsilon)
    )
    return (cross_f32.astype(jnp.bfloat16), coherence)


def gather_by_all_to_all(x, axis, size):
    return lax.all_to_all(jnp.broadcast_to(x, (size,) + x.shape[1:]), axis, 0, 0, tiled=True)


def body(metrics, band_starts):
    row_count = metrics.shape[0]
    local_minutes = metrics.shape[1]
    n_tm = lax.axis_size("tm")
    n_svc = lax.axis_size("svc")
    owners = n_svc // n_tm
    width = BANDS * 2 * BINS
    chunk = width // n_tm
    time_index = lax.axis_index("tm")
    dft_table = make_table(time_index * local_minutes, local_minutes, band_starts)
    dft_table = dft_table.reshape(local_minutes, n_tm, chunk)
    partial_value = jnp.einsum(
        "nt,tcb->cnb", metrics, dft_table, preferred_element_type=jnp.float32
    )
    partials = lax.all_to_all(partial_value, "tm", 0, 0, tiled=True)
    piece = jnp.sum(partials, axis=0, keepdims=True).astype(jnp.bfloat16)
    perm = []
    for s_src in range(n_svc):
        g_src, r_src = divmod(s_src, owners)
        for t_src in range(n_tm):
            s_dst = t_src * owners + r_src
            t_dst = g_src
            perm.append((s_src * n_tm + t_src, s_dst * n_tm + t_dst))
    moved = lax.ppermute(piece, ("svc", "tm"), perm)
    row_chunks = gather_by_all_to_all(piece, "tm", n_tm)
    col_chunks = gather_by_all_to_all(moved, "svc", n_svc)
    bands_row = row_chunks.reshape(BANDS, 2, row_count, BINS)
    row_spec = jnp.transpose(bands_row, (0, 2, 1, 3)).reshape(BANDS, row_count, 2 * BINS)
    bands_col = col_chunks.reshape(BANDS, 2, owners, row_count, BINS)
    col_spec = jnp.transpose(bands_col, (0, 2, 3, 1, 4)).reshape(BANDS, owners * row_count, 2 * BINS)
    return all_bands(row_spec, col_spec)


def solution(mesh):
    return jax.shard_map(
        body,
        mesh=mesh,
        in_specs=(P("svc", "tm"), P()),
        out_specs=(P(None, None, "svc", "tm"), P(None, "svc", "tm")),
        check_vma=False,
    )
```

```python
import jax
import jax.numpy as jnp
from jax import lax
from jax.sharding import PartitionSpec as P

TLEN = 4096
BANDS = 4
BINS = 32


epsilon = 1e-06


def make_table(minutes, band_starts):
    offsets = jnp.arange(BINS, dtype=jnp.int32)
    freqs = band_starts[:, None] + offsets[None, :]
    phase_index = minutes[:, None, None] * freqs[None, :, :] % TLEN
    phases = 2.0 * jnp.pi / TLEN * phase_index.astype(jnp.float32)
    norm = 1.0 / jnp.sqrt(jnp.float32(TLEN))
    stacked = jnp.stack([jnp.cos(phases) * norm, -jnp.sin(phases) * norm], axis=2)
    return stacked.reshape(minutes.shape[0], BANDS * 2 * BINS).astype(jnp.bfloat16)


def all_bands(row_spec, col_spec):
    swapped = jnp.concatenate([row_spec[..., BINS:], -row_spec[..., :BINS]], axis=-1)
    lhs = jnp.stack([row_spec, swapped], axis=1)
    cross_f32 = jnp.einsum("bpik,bjk->bpij", lhs, col_spec, preferred_element_type=jnp.float32) / BINS
    row_power = jnp.sum(jnp.square(row_spec.astype(jnp.float32)), axis=-1) / BINS
    col_power = jnp.sum(jnp.square(col_spec.astype(jnp.float32)), axis=-1) / BINS
    real_part = cross_f32[:, 0]
    imag_part = cross_f32[:, 1]
    coherence = (real_part * real_part + imag_part * imag_part) / (
        (row_power[:, :, None] + epsilon) * (col_power[:, None, :] + epsilon)
    )
    return (cross_f32.astype(jnp.bfloat16), coherence)


def gather_by_all_to_all(x, axis, size):
    return lax.all_to_all(jnp.broadcast_to(x, (size,) + x.shape[1:]), axis, 0, 0, tiled=True)


def body(metrics, band_starts):
    row_count = metrics.shape[0]
    local_minutes = metrics.shape[1]
    n_tm = lax.axis_size("tm")
    n_svc = lax.axis_size("svc")
    owners = n_svc // n_tm
    width = BANDS * 2 * BINS
    chunk = width // n_tm
    time_index = lax.axis_index("tm")
    minutes = time_index * local_minutes + jnp.arange(local_minutes, dtype=jnp.int32)
    dft_table = make_table(minutes, band_starts).reshape(local_minutes, n_tm, chunk)
    partial_value = jnp.einsum(
        "nt,tcb->cnb", metrics, dft_table, preferred_element_type=jnp.float32
    )
    partials = lax.all_to_all(partial_value, "tm", 0, 0, tiled=True)
    piece = jnp.sum(partials, axis=0, keepdims=True).astype(jnp.bfloat16)
    perm = []
    for s_src in range(n_svc):
        g_src, r_src = divmod(s_src, owners)
        for t_src in range(n_tm):
            s_dst = t_src * owners + r_src
            t_dst = g_src
            perm.append((s_src * n_tm + t_src, s_dst * n_tm + t_dst))
    moved = lax.ppermute(piece, ("svc", "tm"), perm)
    row_parts = [piece]
    for shift in range(1, n_tm):
        pairs = [(a * n_tm + b, a * n_tm + (b + shift) % n_tm) for a in range(n_svc) for b in range(n_tm)]
        row_parts.append(lax.ppermute(piece, ("svc", "tm"), pairs))
    order = (time_index - jnp.arange(n_tm, dtype=jnp.int32)) % n_tm
    row_chunks = jnp.take(jnp.concatenate(row_parts, axis=0), order, axis=0)
    col_chunks = gather_by_all_to_all(moved, "svc", n_svc)
    bands_row = row_chunks.reshape(BANDS, 2, row_count, BINS)
    row_spec = jnp.transpose(bands_row, (0, 2, 1, 3)).reshape(BANDS, row_count, 2 * BINS)
    bands_col = col_chunks.reshape(BANDS, 2, owners, row_count, BINS)
    col_spec = jnp.transpose(bands_col, (0, 2, 3, 1, 4)).reshape(BANDS, owners * row_count, 2 * BINS)
    return all_bands(row_spec, col_spec)


def solution(mesh):
    return jax.shard_map(
        body,
        mesh=mesh,
        in_specs=(P("svc", "tm"), P()),
        out_specs=(P(None, None, "svc", "tm"), P(None, "svc", "tm")),
        check_vma=False,
    )
```

```python
import jax
import jax.numpy as jnp
from jax import lax
from jax.sharding import PartitionSpec as P

TLEN = 4096
BANDS = 4
BINS = 32


epsilon = 1e-06


def make_table(minutes, band_starts):
    offsets = jnp.arange(BINS, dtype=jnp.int32)
    freqs = band_starts[:, None] + offsets[None, :]
    phase_index = minutes[:, None, None] * freqs[None, :, :] % TLEN
    phases = 2.0 * jnp.pi / TLEN * phase_index.astype(jnp.float32)
    norm = 1.0 / jnp.sqrt(jnp.float32(TLEN))
    stacked = jnp.stack([jnp.cos(phases) * norm, -jnp.sin(phases) * norm], axis=2)
    return stacked.reshape(minutes.shape[0], BANDS * 2 * BINS).astype(jnp.bfloat16)


def all_bands(row_spec, col_spec):
    swapped = jnp.concatenate([row_spec[..., BINS:], -row_spec[..., :BINS]], axis=-1)
    lhs = jnp.stack([row_spec, swapped], axis=1)
    cross_f32 = jnp.einsum("bpik,bjk->bpij", lhs, col_spec, preferred_element_type=jnp.float32) / BINS
    row_power = jnp.sum(jnp.square(row_spec.astype(jnp.float32)), axis=-1) / BINS
    col_power = jnp.sum(jnp.square(col_spec.astype(jnp.float32)), axis=-1) / BINS
    real_part = cross_f32[:, 0]
    imag_part = cross_f32[:, 1]
    coherence = (real_part * real_part + imag_part * imag_part) / (
        (row_power[:, :, None] + epsilon) * (col_power[:, None, :] + epsilon)
    )
    return (cross_f32.astype(jnp.bfloat16), coherence)


def gather_by_all_to_all(x, axis, size):
    return lax.all_to_all(jnp.broadcast_to(x, (size,) + x.shape[1:]), axis, 0, 0, tiled=True)


def body(metrics, band_starts):
    row_count = metrics.shape[0]
    local_minutes = metrics.shape[1]
    n_tm = lax.axis_size("tm")
    n_svc = lax.axis_size("svc")
    owners = n_svc // n_tm
    width = BANDS * 2 * BINS
    chunk = width // n_tm
    time_index = lax.axis_index("tm")
    minutes = time_index * local_minutes + jnp.arange(local_minutes, dtype=jnp.int32)
    dft_table = make_table(minutes, band_starts).reshape(local_minutes, n_tm, chunk)
    partial_value = jnp.einsum(
        "nt,tcb->cnb", metrics, dft_table, preferred_element_type=jnp.float32
    )
    partials = lax.all_to_all(partial_value, "tm", 0, 0, tiled=True)
    piece = jnp.sum(partials, axis=0, keepdims=True).astype(jnp.bfloat16)
    perm = []
    for s_src in range(n_svc):
        g_src, r_src = divmod(s_src, owners)
        for t_src in range(n_tm):
            s_dst = t_src * owners + r_src
            t_dst = g_src
            perm.append((s_src * n_tm + t_src, s_dst * n_tm + t_dst))
    moved = lax.ppermute(piece, ("svc", "tm"), perm)
    row_chunks = piece
    distance = 1
    while distance < n_tm:
        pairs = [(a * n_tm + b, a * n_tm + (b ^ distance)) for a in range(n_svc) for b in range(n_tm)]
        received = lax.ppermute(row_chunks, ("svc", "tm"), pairs)
        upper = (time_index & distance) != 0
        row_chunks = jnp.where(
            upper,
            jnp.concatenate([received, row_chunks], axis=0),
            jnp.concatenate([row_chunks, received], axis=0),
        )
        distance *= 2
    col_chunks = gather_by_all_to_all(moved, "svc", n_svc)
    bands_row = row_chunks.reshape(BANDS, 2, row_count, BINS)
    row_spec = jnp.transpose(bands_row, (0, 2, 1, 3)).reshape(BANDS, row_count, 2 * BINS)
    bands_col = col_chunks.reshape(BANDS, 2, owners, row_count, BINS)
    col_spec = jnp.transpose(bands_col, (0, 2, 3, 1, 4)).reshape(BANDS, owners * row_count, 2 * BINS)
    return all_bands(row_spec, col_spec)


def solution(mesh):
    return jax.shard_map(
        body,
        mesh=mesh,
        in_specs=(P("svc", "tm"), P()),
        out_specs=(P(None, None, "svc", "tm"), P(None, "svc", "tm")),
        check_vma=False,
    )
```

```python
import jax
import jax.numpy as jnp
from jax import lax
from jax.sharding import PartitionSpec as P

TLEN = 4096
BANDS = 4
BINS = 32


epsilon = 1e-06


def make_table(minutes, band_starts):
    offsets = jnp.arange(BINS, dtype=jnp.int32)
    freqs = band_starts[:, None] + offsets[None, :]
    phase_index = minutes[:, None, None] * freqs[None, :, :] % TLEN
    phases = 2.0 * jnp.pi / TLEN * phase_index.astype(jnp.float32)
    norm = 1.0 / jnp.sqrt(jnp.float32(TLEN))
    stacked = jnp.stack([jnp.cos(phases) * norm, -jnp.sin(phases) * norm], axis=2)
    return stacked.reshape(minutes.shape[0], BANDS * 2 * BINS).astype(jnp.bfloat16)


def all_bands(row_spec, col_spec):
    swapped = jnp.concatenate([row_spec[..., BINS:], -row_spec[..., :BINS]], axis=-1)
    lhs = jnp.stack([row_spec, swapped], axis=1)
    cross_f32 = jnp.einsum("bpik,bjk->bpij", lhs, col_spec, preferred_element_type=jnp.float32) / BINS
    row_power = jnp.sum(jnp.square(row_spec.astype(jnp.float32)), axis=-1) / BINS
    col_power = jnp.sum(jnp.square(col_spec.astype(jnp.float32)), axis=-1) / BINS
    real_part = cross_f32[:, 0]
    imag_part = cross_f32[:, 1]
    coherence = (real_part * real_part + imag_part * imag_part) / (
        (row_power[:, :, None] + epsilon) * (col_power[:, None, :] + epsilon)
    )
    return (cross_f32.astype(jnp.bfloat16), coherence)


def gather_by_all_to_all(x, axis, size):
    return lax.all_to_all(jnp.broadcast_to(x, (size,) + x.shape[1:]), axis, 0, 0, tiled=True)


def body(metrics, band_starts):
    row_count = metrics.shape[0]
    local_minutes = metrics.shape[1]
    n_tm = lax.axis_size("tm")
    n_svc = lax.axis_size("svc")
    owners = n_svc // n_tm
    width = BANDS * 2 * BINS
    chunk = width // n_tm
    time_index = lax.axis_index("tm")
    minutes = time_index * local_minutes + jnp.arange(local_minutes, dtype=jnp.int32)
    dft_table = make_table(minutes, band_starts).reshape(local_minutes, n_tm, chunk)
    partial_value = jnp.einsum(
        "nt,tcb->cnb", metrics, dft_table, preferred_element_type=jnp.float32
    )
    held = partial_value
    distance = n_tm // 2
    while distance >= 1:
        half = held.shape[0] // 2
        upper = ((time_index & distance) != 0).astype(jnp.int32)
        kept = lax.dynamic_slice_in_dim(held, upper * half, half, 0)
        sent = lax.dynamic_slice_in_dim(held, (1 - upper) * half, half, 0)
        pairs = [(a * n_tm + b, a * n_tm + (b ^ distance)) for a in range(n_svc) for b in range(n_tm)]
        held = kept + lax.ppermute(sent, ("svc", "tm"), pairs)
        distance //= 2
    piece = held.astype(jnp.bfloat16)
    perm = []
    for s_src in range(n_svc):
        g_src, r_src = divmod(s_src, owners)
        for t_src in range(n_tm):
            s_dst = t_src * owners + r_src
            t_dst = g_src
            perm.append((s_src * n_tm + t_src, s_dst * n_tm + t_dst))
    moved = lax.ppermute(piece, ("svc", "tm"), perm)
    row_chunks = piece
    distance = 1
    while distance < n_tm:
        pairs = [(a * n_tm + b, a * n_tm + (b ^ distance)) for a in range(n_svc) for b in range(n_tm)]
        received = lax.ppermute(row_chunks, ("svc", "tm"), pairs)
        upper = (time_index & distance) != 0
        row_chunks = jnp.where(
            upper,
            jnp.concatenate([received, row_chunks], axis=0),
            jnp.concatenate([row_chunks, received], axis=0),
        )
        distance *= 2
    col_chunks = gather_by_all_to_all(moved, "svc", n_svc)
    bands_row = row_chunks.reshape(BANDS, 2, row_count, BINS)
    row_spec = jnp.transpose(bands_row, (0, 2, 1, 3)).reshape(BANDS, row_count, 2 * BINS)
    bands_col = col_chunks.reshape(BANDS, 2, owners, row_count, BINS)
    col_spec = jnp.transpose(bands_col, (0, 2, 3, 1, 4)).reshape(BANDS, owners * row_count, 2 * BINS)
    return all_bands(row_spec, col_spec)


def solution(mesh):
    return jax.shard_map(
        body,
        mesh=mesh,
        in_specs=(P("svc", "tm"), P()),
        out_specs=(P(None, None, "svc", "tm"), P(None, "svc", "tm")),
        check_vma=False,
    )
```

```python
import jax
import jax.numpy as jnp
from jax import lax
from jax.sharding import PartitionSpec as P

TLEN = 4096
BANDS = 4
BINS = 32


epsilon = 1e-06


def make_table(minutes, band_starts):
    offsets = jnp.arange(BINS, dtype=jnp.int32)
    freqs = band_starts[:, None] + offsets[None, :]
    phase_index = minutes[:, None, None] * freqs[None, :, :] % TLEN
    phases = 2.0 * jnp.pi / TLEN * phase_index.astype(jnp.float32)
    norm = 1.0 / jnp.sqrt(jnp.float32(TLEN))
    stacked = jnp.stack([jnp.cos(phases) * norm, -jnp.sin(phases) * norm], axis=2)
    return stacked.reshape(minutes.shape[0], BANDS * 2 * BINS).astype(jnp.bfloat16)


def all_bands(row_spec, col_spec):
    swapped = jnp.concatenate([row_spec[..., BINS:], -row_spec[..., :BINS]], axis=-1)
    lhs = jnp.stack([row_spec, swapped], axis=1)
    cross_f32 = jnp.einsum("bpik,bjk->bpij", lhs, col_spec, preferred_element_type=jnp.float32) / BINS
    row_power = jnp.sum(jnp.square(row_spec.astype(jnp.float32)), axis=-1) / BINS
    col_power = jnp.sum(jnp.square(col_spec.astype(jnp.float32)), axis=-1) / BINS
    real_part = cross_f32[:, 0]
    imag_part = cross_f32[:, 1]
    coherence = (real_part * real_part + imag_part * imag_part) / (
        (row_power[:, :, None] + epsilon) * (col_power[:, None, :] + epsilon)
    )
    return (cross_f32.astype(jnp.bfloat16), coherence)


def gather_by_all_to_all(x, axis, size):
    return lax.all_to_all(jnp.broadcast_to(x, (size,) + x.shape[1:]), axis, 0, 0, tiled=True)


def body(metrics, band_starts):
    row_count = metrics.shape[0]
    local_minutes = metrics.shape[1]
    n_tm = lax.axis_size("tm")
    n_svc = lax.axis_size("svc")
    owners = n_svc // n_tm
    width = BANDS * 2 * BINS
    chunk = width // n_tm
    time_index = lax.axis_index("tm")
    minutes = time_index * local_minutes + jnp.arange(local_minutes, dtype=jnp.int32)
    dft_table = make_table(minutes, band_starts).reshape(local_minutes, n_tm, chunk)
    partial_value = jnp.einsum(
        "nt,tcb->cnb", metrics, dft_table, preferred_element_type=jnp.float32
    )
    span = n_tm // 2
    groups = partial_value.reshape(n_tm // span, span, row_count, chunk)
    outgoing = jnp.repeat(groups, span, axis=0)
    partials = lax.all_to_all(outgoing, "tm", 0, 0, tiled=True)
    own_group = jnp.sum(partials, axis=0).astype(jnp.bfloat16)
    piece = lax.dynamic_slice_in_dim(own_group, time_index % span, 1, 0)
    perm = []
    for s_src in range(n_svc):
        g_src, r_src = divmod(s_src, owners)
        for t_src in range(n_tm):
            s_dst = t_src * owners + r_src
            t_dst = g_src
            perm.append((s_src * n_tm + t_src, s_dst * n_tm + t_dst))
    moved = lax.ppermute(piece, ("svc", "tm"), perm)
    pairs = [(a * n_tm + b, a * n_tm + (b ^ span)) for a in range(n_svc) for b in range(n_tm)]
    received = lax.ppermute(own_group, ("svc", "tm"), pairs)
    upper = (time_index & span) != 0
    row_chunks = jnp.where(
        upper,
        jnp.concatenate([received, own_group], axis=0),
        jnp.concatenate([own_group, received], axis=0),
    )
    col_chunks = gather_by_all_to_all(moved, "svc", n_svc)
    bands_row = row_chunks.reshape(BANDS, 2, row_count, BINS)
    row_spec = jnp.transpose(bands_row, (0, 2, 1, 3)).reshape(BANDS, row_count, 2 * BINS)
    bands_col = col_chunks.reshape(BANDS, 2, owners, row_count, BINS)
    col_spec = jnp.transpose(bands_col, (0, 2, 3, 1, 4)).reshape(BANDS, owners * row_count, 2 * BINS)
    return all_bands(row_spec, col_spec)


def solution(mesh):
    return jax.shard_map(
        body,
        mesh=mesh,
        in_specs=(P("svc", "tm"), P()),
        out_specs=(P(None, None, "svc", "tm"), P(None, "svc", "tm")),
        check_vma=False,
    )
```

```python
import jax
import jax.numpy as jnp
from jax import lax
from jax.sharding import PartitionSpec as P

TLEN = 4096
BANDS = 4
BINS = 32


epsilon = 1e-06


def make_table(minutes, band_starts):
    offsets = jnp.arange(BINS, dtype=jnp.int32)
    freqs = band_starts[:, None] + offsets[None, :]
    phase_index = minutes[:, None, None] * freqs[None, :, :] % TLEN
    phases = 2.0 * jnp.pi / TLEN * phase_index.astype(jnp.float32)
    norm = 1.0 / jnp.sqrt(jnp.float32(TLEN))
    stacked = jnp.stack([jnp.cos(phases) * norm, -jnp.sin(phases) * norm], axis=2)
    return stacked.reshape(minutes.shape[0], BANDS * 2 * BINS).astype(jnp.bfloat16)


def all_bands(row_spec, col_spec):
    swapped = jnp.concatenate([row_spec[..., BINS:], -row_spec[..., :BINS]], axis=-1)
    lhs = jnp.stack([row_spec, swapped], axis=1)
    cross_f32 = jnp.einsum("bpik,bjk->bpij", lhs, col_spec, preferred_element_type=jnp.float32) / BINS
    row_power = jnp.sum(jnp.square(row_spec.astype(jnp.float32)), axis=-1) / BINS
    col_power = jnp.sum(jnp.square(col_spec.astype(jnp.float32)), axis=-1) / BINS
    real_part = cross_f32[:, 0]
    imag_part = cross_f32[:, 1]
    coherence = (real_part * real_part + imag_part * imag_part) / (
        (row_power[:, :, None] + epsilon) * (col_power[:, None, :] + epsilon)
    )
    return (cross_f32.astype(jnp.bfloat16), coherence)


def gather_by_all_to_all(x, axis, size):
    return lax.all_to_all(jnp.broadcast_to(x, (size,) + x.shape[1:]), axis, 0, 0, tiled=True)


def body(metrics, band_starts):
    row_count = metrics.shape[0]
    local_minutes = metrics.shape[1]
    n_tm = lax.axis_size(TM)
    n_svc = lax.axis_size("svc")
    owners = n_svc // n_tm
    width = BANDS * 2 * BINS
    chunk = width // n_tm
    time_index = lax.axis_index(TM)
    minutes = time_index * local_minutes + jnp.arange(local_minutes, dtype=jnp.int32)
    dft_table = make_table(minutes, band_starts).reshape(local_minutes, n_tm, chunk)
    partial_value = jnp.einsum(
        "nt,tcb->cnb", metrics, dft_table, preferred_element_type=jnp.float32
    )
    partials = lax.all_to_all(partial_value, TM, 0, 0, tiled=True)
    piece = jnp.sum(partials, axis=0, keepdims=True).astype(jnp.bfloat16)
    perm = []
    for s_src in range(n_svc):
        g_src, r_src = divmod(s_src, owners)
        for t_src in range(n_tm):
            s_dst = t_src * owners + r_src
            t_dst = g_src
            perm.append((s_src * n_tm + t_src, s_dst * n_tm + t_dst))
    moved = lax.ppermute(piece, ("svc",) + TM, perm)
    near = lax.axis_size("x")
    own_group = gather_by_all_to_all(piece, "x", near)
    pairs = [(a * n_tm + b, a * n_tm + (b ^ near)) for a in range(n_svc) for b in range(n_tm)]
    received = lax.ppermute(own_group, ("svc",) + TM, pairs)
    upper = (time_index & near) != 0
    row_chunks = jnp.where(
        upper,
        jnp.concatenate([received, own_group], axis=0),
        jnp.concatenate([own_group, received], axis=0),
    )
    col_chunks = gather_by_all_to_all(moved, "svc", n_svc)
    bands_row = row_chunks.reshape(BANDS, 2, row_count, BINS)
    row_spec = jnp.transpose(bands_row, (0, 2, 1, 3)).reshape(BANDS, row_count, 2 * BINS)
    bands_col = col_chunks.reshape(BANDS, 2, owners, row_count, BINS)
    col_spec = jnp.transpose(bands_col, (0, 2, 3, 1, 4)).reshape(BANDS, owners * row_count, 2 * BINS)
    return all_bands(row_spec, col_spec)


TM = ("far", "x")


def solution(mesh):
    n_svc, n_tm = mesh.shape["svc"], mesh.shape["tm"]
    n_x = 4 if n_tm % 4 == 0 else n_tm
    split = jax.sharding.Mesh(mesh.devices.reshape(n_svc, n_tm // n_x, n_x), ("svc",) + TM)
    return jax.shard_map(
        body,
        mesh=split,
        in_specs=(P("svc", TM), P()),
        out_specs=(P(None, None, "svc", TM), P(None, "svc", TM)),
        check_vma=False,
    )
```

```python
import jax
import jax.numpy as jnp
from jax import lax
from jax.sharding import PartitionSpec as P

TLEN = 4096
BANDS = 4
BINS = 32


epsilon = 1e-06


def make_table(minutes, band_starts):
    offsets = jnp.arange(BINS, dtype=jnp.int32)
    freqs = band_starts[:, None] + offsets[None, :]
    phase_index = minutes[:, None, None] * freqs[None, :, :] % TLEN
    phases = 2.0 * jnp.pi / TLEN * phase_index.astype(jnp.float32)
    norm = 1.0 / jnp.sqrt(jnp.float32(TLEN))
    stacked = jnp.stack([jnp.cos(phases) * norm, -jnp.sin(phases) * norm], axis=2)
    return stacked.reshape(minutes.shape[0], BANDS * 2 * BINS).astype(jnp.bfloat16)


def all_bands(row_spec, col_spec):
    swapped = jnp.concatenate([row_spec[..., BINS:], -row_spec[..., :BINS]], axis=-1)
    lhs = jnp.stack([row_spec, swapped], axis=1)
    cross_f32 = jnp.einsum("bpik,bjk->bpij", lhs, col_spec, preferred_element_type=jnp.float32) / BINS
    row_power = jnp.sum(jnp.square(row_spec.astype(jnp.float32)), axis=-1) / BINS
    col_power = jnp.sum(jnp.square(col_spec.astype(jnp.float32)), axis=-1) / BINS
    real_part = cross_f32[:, 0]
    imag_part = cross_f32[:, 1]
    coherence = (real_part * real_part + imag_part * imag_part) / (
        (row_power[:, :, None] + epsilon) * (col_power[:, None, :] + epsilon)
    )
    return (cross_f32.astype(jnp.bfloat16), coherence)


def gather_by_all_to_all(x, axis, size):
    return lax.all_to_all(jnp.broadcast_to(x, (size,) + x.shape[1:]), axis, 0, 0, tiled=True)


def body(metrics, band_starts):
    row_count = metrics.shape[0]
    local_minutes = metrics.shape[1]
    n_tm = lax.axis_size("tm")
    n_svc = lax.axis_size("svc")
    owners = n_svc // n_tm
    width = BANDS * 2 * BINS
    chunk = width // n_tm
    time_index = lax.axis_index("tm")
    minutes = time_index * local_minutes + jnp.arange(local_minutes, dtype=jnp.int32)
    dft_table = make_table(minutes, band_starts).reshape(local_minutes, n_tm, chunk)
    partial_value = jnp.einsum(
        "nt,tcb->cnb", metrics, dft_table, preferred_element_type=jnp.float32
    )
    partials = lax.all_to_all(partial_value, "tm", 0, 0, tiled=True)
    piece = jnp.sum(partials, axis=0, keepdims=True).astype(jnp.bfloat16)
    every_block = gather_by_all_to_all(piece, "svc", n_svc)
    panel = every_block.reshape(n_tm, owners, row_count, chunk)
    own = jnp.broadcast_to(piece[None], (n_tm, 1, row_count, chunk))
    received = lax.all_to_all(jnp.concatenate([panel, own], axis=1), "tm", 0, 0, tiled=True)
    row_chunks = received[:, owners]
    col_chunks = received[:, :owners].reshape(n_svc, row_count, chunk)
    bands_row = row_chunks.reshape(BANDS, 2, row_count, BINS)
    row_spec = jnp.transpose(bands_row, (0, 2, 1, 3)).reshape(BANDS, row_count, 2 * BINS)
    bands_col = col_chunks.reshape(BANDS, 2, owners, row_count, BINS)
    col_spec = jnp.transpose(bands_col, (0, 2, 3, 1, 4)).reshape(BANDS, owners * row_count, 2 * BINS)
    return all_bands(row_spec, col_spec)


def solution(mesh):
    return jax.shard_map(
        body,
        mesh=mesh,
        in_specs=(P("svc", "tm"), P()),
        out_specs=(P(None, None, "svc", "tm"), P(None, "svc", "tm")),
        check_vma=False,
    )
```

```python
import jax
import jax.numpy as jnp
from jax import lax
from jax.sharding import PartitionSpec as P

TLEN = 4096
BANDS = 4
BINS = 32


epsilon = 1e-06


def make_table(minutes, band_starts):
    offsets = jnp.arange(BINS, dtype=jnp.int32)
    freqs = band_starts[:, None] + offsets[None, :]
    phase_index = minutes[:, None, None] * freqs[None, :, :] % TLEN
    phases = 2.0 * jnp.pi / TLEN * phase_index.astype(jnp.float32)
    norm = 1.0 / jnp.sqrt(jnp.float32(TLEN))
    stacked = jnp.stack([jnp.cos(phases) * norm, -jnp.sin(phases) * norm], axis=2)
    return stacked.reshape(minutes.shape[0], BANDS * 2 * BINS).astype(jnp.bfloat16)


def all_bands(row_spec, col_spec):
    swapped = jnp.concatenate([row_spec[..., BINS:], -row_spec[..., :BINS]], axis=-1)
    lhs = jnp.stack([row_spec, swapped], axis=1)
    cross_f32 = jnp.einsum("bpik,bjk->bpij", lhs, col_spec, preferred_element_type=jnp.float32) / BINS
    row_power = jnp.sum(jnp.square(row_spec.astype(jnp.float32)), axis=-1) / BINS
    col_power = jnp.sum(jnp.square(col_spec.astype(jnp.float32)), axis=-1) / BINS
    real_part = cross_f32[:, 0]
    imag_part = cross_f32[:, 1]
    coherence = (real_part * real_part + imag_part * imag_part) / (
        (row_power[:, :, None] + epsilon) * (col_power[:, None, :] + epsilon)
    )
    return (cross_f32.astype(jnp.bfloat16), coherence)


def gather_by_all_to_all(x, axis, size):
    return lax.all_to_all(jnp.broadcast_to(x, (size,) + x.shape[1:]), axis, 0, 0, tiled=True)


def body(metrics, band_starts):
    row_count = metrics.shape[0]
    local_minutes = metrics.shape[1]
    n_tm = lax.axis_size("tm")
    n_svc = lax.axis_size("svc")
    owners = n_svc // n_tm
    width = BANDS * 2 * BINS
    chunk = width // n_tm
    time_index = lax.axis_index("tm")
    minutes = time_index * local_minutes + jnp.arange(local_minutes, dtype=jnp.int32)
    dft_table = make_table(minutes, band_starts).reshape(local_minutes, n_tm, chunk)
    partial_value = jnp.einsum(
        "nt,tcb->cnb", metrics, dft_table, preferred_element_type=jnp.float32
    )
    partials = lax.all_to_all(partial_value, "tm", 0, 0, tiled=True)
    piece = jnp.sum(partials, axis=0, keepdims=True).astype(jnp.bfloat16)
    perm = []
    for s_src in range(n_svc):
        g_src, r_src = divmod(s_src, owners)
        for t_src in range(n_tm):
            s_dst = t_src * owners + r_src
            t_dst = g_src
            perm.append((s_src * n_tm + t_src, s_dst * n_tm + t_dst))
    moved = lax.ppermute(piece, ("svc", "tm"), perm)
    row_chunks = piece
    distance = n_tm // 2
    while distance >= 1:
        pairs = [(a * n_tm + b, a * n_tm + (b ^ distance)) for a in range(n_svc) for b in range(n_tm)]
        received = lax.ppermute(row_chunks, ("svc", "tm"), pairs)
        upper = (time_index & distance) != 0
        row_chunks = jnp.where(
            upper,
            jnp.stack([received, row_chunks], axis=1),
            jnp.stack([row_chunks, received], axis=1),
        ).reshape((2 * row_chunks.shape[0],) + piece.shape[1:])
        distance //= 2
    col_chunks = gather_by_all_to_all(moved, "svc", n_svc)
    bands_row = row_chunks.reshape(BANDS, 2, row_count, BINS)
    row_spec = jnp.transpose(bands_row, (0, 2, 1, 3)).reshape(BANDS, row_count, 2 * BINS)
    bands_col = col_chunks.reshape(BANDS, 2, owners, row_count, BINS)
    col_spec = jnp.transpose(bands_col, (0, 2, 3, 1, 4)).reshape(BANDS, owners * row_count, 2 * BINS)
    return all_bands(row_spec, col_spec)


def solution(mesh):
    return jax.shard_map(
        body,
        mesh=mesh,
        in_specs=(P("svc", "tm"), P()),
        out_specs=(P(None, None, "svc", "tm"), P(None, "svc", "tm")),
        check_vma=False,
    )
```

```python
import jax
import jax.numpy as jnp
from jax import lax
from jax.sharding import PartitionSpec as P

TLEN = 4096
BANDS = 4
BINS = 32


epsilon = 1e-06


def make_table(minutes, band_starts):
    offsets = jnp.arange(BINS, dtype=jnp.int32)
    freqs = band_starts[:, None] + offsets[None, :]
    phase_index = minutes[:, None, None] * freqs[None, :, :] % TLEN
    phases = 2.0 * jnp.pi / TLEN * phase_index.astype(jnp.float32)
    norm = 1.0 / jnp.sqrt(jnp.float32(TLEN))
    stacked = jnp.stack([jnp.cos(phases) * norm, -jnp.sin(phases) * norm], axis=2)
    return stacked.reshape(minutes.shape[0], BANDS * 2 * BINS).astype(jnp.bfloat16)


def all_bands(row_spec, col_spec):
    swapped = jnp.concatenate([row_spec[..., BINS:], -row_spec[..., :BINS]], axis=-1)
    lhs = jnp.stack([row_spec, swapped], axis=1)
    cross_f32 = jnp.einsum("bpik,bjk->bpij", lhs, col_spec, preferred_element_type=jnp.float32) / BINS
    row_power = jnp.sum(jnp.square(row_spec.astype(jnp.float32)), axis=-1) / BINS
    col_power = jnp.sum(jnp.square(col_spec.astype(jnp.float32)), axis=-1) / BINS
    real_part = cross_f32[:, 0]
    imag_part = cross_f32[:, 1]
    coherence = (real_part * real_part + imag_part * imag_part) / (
        (row_power[:, :, None] + epsilon) * (col_power[:, None, :] + epsilon)
    )
    return (cross_f32.astype(jnp.bfloat16), coherence)


def gather_by_all_to_all(x, axis, size):
    return lax.all_to_all(jnp.broadcast_to(x, (size,) + x.shape[1:]), axis, 0, 0, tiled=True)


def body(metrics, band_starts):
    row_count = metrics.shape[0]
    local_minutes = metrics.shape[1]
    n_tm = lax.axis_size("tm")
    n_svc = lax.axis_size("svc")
    owners = n_svc // n_tm
    width = BANDS * 2 * BINS
    chunk = width // n_tm
    time_index = lax.axis_index("tm")
    minutes = time_index * local_minutes + jnp.arange(local_minutes, dtype=jnp.int32)
    dft_table = make_table(minutes, band_starts).reshape(local_minutes, n_tm, chunk)
    partial_value = jnp.einsum(
        "nt,tcb->cnb", metrics, dft_table, preferred_element_type=jnp.float32
    )
    far = n_tm // 2
    pairs_of = jnp.swapaxes(partial_value.reshape(2, far, row_count, chunk), 0, 1)
    partials = lax.all_to_all(jnp.concatenate([pairs_of, pairs_of], axis=0), "tm", 0, 0, tiled=True)
    own_pair = jnp.sum(partials, axis=0).astype(jnp.bfloat16)
    piece = lax.dynamic_slice_in_dim(own_pair, time_index // far, 1, 0)
    perm = []
    for s_src in range(n_svc):
        g_src, r_src = divmod(s_src, owners)
        for t_src in range(n_tm):
            s_dst = t_src * owners + r_src
            t_dst = g_src
            perm.append((s_src * n_tm + t_src, s_dst * n_tm + t_dst))
    moved = lax.ppermute(piece, ("svc", "tm"), perm)
    row_chunks = own_pair
    distance = far // 2
    while distance >= 1:
        pairs = [(a * n_tm + b, a * n_tm + (b ^ distance)) for a in range(n_svc) for b in range(n_tm)]
        received = lax.ppermute(row_chunks, ("svc", "tm"), pairs)
        upper = (time_index & distance) != 0
        row_chunks = jnp.where(
            upper,
            jnp.stack([received, row_chunks], axis=1),
            jnp.stack([row_chunks, received], axis=1),
        ).reshape((2 * row_chunks.shape[0],) + piece.shape[1:])
        distance //= 2
    col_chunks = gather_by_all_to_all(moved, "svc", n_svc)
    bands_row = row_chunks.reshape(BANDS, 2, row_count, BINS)
    row_spec = jnp.transpose(bands_row, (0, 2, 1, 3)).reshape(BANDS, row_count, 2 * BINS)
    bands_col = col_chunks.reshape(BANDS, 2, owners, row_count, BINS)
    col_spec = jnp.transpose(bands_col, (0, 2, 3, 1, 4)).reshape(BANDS, owners * row_count, 2 * BINS)
    return all_bands(row_spec, col_spec)


def solution(mesh):
    return jax.shard_map(
        body,
        mesh=mesh,
        in_specs=(P("svc", "tm"), P()),
        out_specs=(P(None, None, "svc", "tm"), P(None, "svc", "tm")),
        check_vma=False,
    )
```
